1024 devices in a mesh: curve: 64 (over y, x), coef: 16 (over z, core).
Axes of the slice: x: 8, y: 8, z: 8, core: 2. Of those that a mesh axis runs over, the one named last changes fastest.
Arguments:
- right_side: float32 [64, 1048576], P(None, ('curve', 'coef'))
- group_ids: int32 [1048576], P(('curve', 'coef')), may hold values from 0 to 8191, as said below
- pair_sources: int32 [8192, 16], P(('curve', 'coef')), may hold values from 0 to 8191, as said below
- pair_weights: float32 [8192, 16], P(('curve', 'coef')), may hold values from 0.3 to 1
- self_diag: float32 [1048576], P(('curve', 'coef')), may hold values from 1 to 4
- self_trans: float32 [64, 64], replicated, may hold values from -0.375 to 0.375
- far_trans: float32 [64, 64], replicated, may hold values from -0.015625 to 0.015625
Outputs:
- solution: float32 [64, 1048576], P(None, ('curve', 'coef'))
The draws below stay inside these ranges and needn't reach their ends.
Inputs may be any that keep to these rules, and one draw needn't show every extreme that they name: `group_ids`: the particles of one device belong to its 8 groups: on device d the ids are non-decreasing and run from 8 * d to 8 * d + 7, first and last reached. `pair_sources`: each listed source group s of target group t has |s - t| <= 8; that distance is reached in every draw.
All inputs are finite; a program needn't handle non-finite values.
Results may differ from the reference program's by a relative error of at most 0.0001.
Values sent between devices are 32-bit elements; how exact they have to be, the bound alone decides.
No kernel may reach another device: no remote copies, remote signals or barrier semaphores. Data moves between devices by JAX's collectives and lax.ppermute only.
A program may use at most 32 MiB of HBM per device.

```python
import math
import jax
import jax.numpy as jnp
from jax import lax

C = 64
PART_DEV = 1024
GSIZE = 128
NB = 16
ITERS = 2
GDEV = 8
PARTICLES = 1048576
NG = 8192


def draw_right_side(key, part):
    position = jnp.arange(PARTICLES, dtype=jnp.float32)[None, :]
    rising = 1.0 + 2.0 * position / PARTICLES
    values = jax.random.normal(key, (C, PARTICLES), jnp.float32) * rising
    return values.astype(jnp.float32)


def draw_group_ids(key, part):
    devices_count = PARTICLES // PART_DEV
    slots = jax.random.randint(key, (devices_count, PART_DEV), 0, GDEV)
    slots = jnp.sort(slots, axis=1)
    slots = slots.at[:, 0].set(0)
    slots = slots.at[:, PART_DEV - 1].set(GDEV - 1)
    offsets = (jnp.arange(devices_count, dtype=jnp.int32) * GDEV)[:, None]
    return (slots + offsets).reshape(PARTICLES).astype(jnp.int32)


def draw_pair_sources(key, part):
    target = jnp.arange(NG, dtype=jnp.int32)[:, None]
    offsets = jax.random.randint(key, (NG, NB), -GDEV, GDEV + 1)
    offsets = offsets.at[:, 0].set(0)
    offsets = offsets.at[:, 1].set(GDEV)
    offsets = offsets.at[:, 2].set(-GDEV)
    return jnp.clip(target + offsets, 0, NG - 1).astype(jnp.int32)


def level_of(stream_key, extent, shards, least, top_value):
    def one(dim, shards_of):
        draws = jax.random.uniform(jax.random.fold_in(jax.random.fold_in(stream_key, 6), dim), (shards_of,), jnp.float32, least / len(shards), top_value / len(shards))
        return jnp.repeat(jnp.exp(draws), extent[dim] // shards_of).reshape((-1,) + (1,) * (len(extent) - dim - 1))

    factor_of = one(*shards[0])
    for cut in shards[1:]:
        factor_of = factor_of * one(*cut)
    return factor_of


def gaussian(stream_key, shape, spread, limit, held_as=jnp.bfloat16):
    return jnp.clip(spread * jax.random.normal(stream_key, shape, jnp.float32), -limit, limit).astype(held_as)


def setup_inputs(seed: int = 0) -> dict:
    keys = jax.random.split(jax.random.key(seed), 8)
    return {
        "right_side": draw_right_side(jax.random.fold_in(keys[7], 71), 0),
        "group_ids": draw_group_ids(jax.random.fold_in(keys[7], 71), 0),
        "pair_sources": draw_pair_sources(jax.random.fold_in(keys[7], 71), 0),
        "pair_weights": jnp.clip(jnp.exp(math.log(1.0) - 1.2039728 * jax.random.uniform(keys[3], (NG, NB), jnp.float32) ** level_of(keys[3], (NG, NB), ((0, 1024),), -0.2, 0.2)), 0.3, 1.0),
        "self_diag": jnp.clip(jnp.exp(math.log(4.0) - 1.3862944 * jax.random.uniform(keys[4], (PARTICLES,), jnp.float32) ** level_of(keys[4], (PARTICLES,), ((0, 1024),), -0.2, 0.2)), 1.0, 4.0),
        "self_trans": gaussian(keys[5], (C, C), (4 * C) ** -0.5, 0.375, jnp.float32),
        "far_trans": gaussian(keys[6], (C, C), (C * GSIZE * NB) ** -0.5, 0.015625, jnp.float32),
    }


def apply_operator(field, group_ids, pair_sources, pair_weights, self_diag, self_trans, far_trans):
    highest = lax.Precision.HIGHEST
    moments = jax.ops.segment_sum(field.T, group_ids, num_segments=NG)
    gathered = lax.optimization_barrier(jnp.sum(pair_weights[:, :, None] * moments[pair_sources], axis=1))
    local = jnp.dot(gathered, far_trans.T, precision=highest)
    return self_diag[None, :] * field + jnp.dot(self_trans, field, precision=highest) + local[group_ids].T

def least_squares(hessen, beta_norm):
    highest = lax.Precision.HIGHEST
    gram_mat = jnp.dot(hessen.T, hessen, precision=highest)
    factor = jnp.linalg.cholesky(gram_mat)
    target = beta_norm * hessen[0]
    forward = []
    for row in range(ITERS):
        value = target[row]
        for col in range(row):
            value = value - factor[row, col] * forward[col]
        forward.append(value / factor[row, row])
    backward = [None] * ITERS
    for row in range(ITERS - 1, -1, -1):
        value = forward[row]
        for col in range(row + 1, ITERS):
            value = value - factor[col, row] * backward[col]
        backward[row] = value / factor[row, row]
    return backward

def reference(right_side, group_ids, pair_sources, pair_weights, self_diag, self_trans, far_trans):
    beta_norm = jnp.sqrt(jnp.sum(right_side * right_side))
    basis = [right_side / beta_norm]
    hessen = jnp.zeros((ITERS + 1, ITERS), jnp.float32)
    for column in range(ITERS):
        image = apply_operator(basis[column], group_ids, pair_sources, pair_weights, self_diag, self_trans, far_trans)
        projections = [jnp.sum(basis[earlier] * image) for earlier in range(column + 1)]
        squared = jnp.sum(image * image)
        lowest = jnp.sqrt(squared - sum((value * value for value in projections)))
        for earlier in range(column + 1):
            hessen = hessen.at[earlier, column].set(projections[earlier])
        hessen = hessen.at[column + 1, column].set(lowest)
        if column < ITERS - 1:
            remainder = image
            for earlier in range(column + 1):
                remainder = remainder - projections[earlier] * basis[earlier]
            basis.append(remainder / lowest)
    coeffs = least_squares(hessen, beta_norm)
    solution = coeffs[0] * basis[0]
    for column in range(1, ITERS):
        solution = solution + coeffs[column] * basis[column]
    return solution
```

```python
import jax
import jax.numpy as jnp
from jax import lax
from jax.sharding import PartitionSpec as P

ITERS = 2
DEVICES = ("curve", "coef")
GRAM_PAIRS = ((0, 0), (0, 1), (0, 2), (1, 1), (1, 2), (2, 2))


def shifted(array, axis, by):
    peers = lax.axis_size(axis)
    pairs = [(i, i + by) for i in range(peers) if 0 <= i + by < peers]
    return lax.ppermute(array, axis, pairs)


def apply_operator(field, slot_table, select_mat, self_diag, self_trans, far_trans):
    highest = lax.Precision.HIGHEST
    moments = jnp.dot(field, slot_table.T, precision=highest)
    lower = shifted(moments, DEVICES, 1)
    upper = shifted(moments, DEVICES, -1)
    extended = jnp.concatenate([lower, moments, upper], axis=1)
    gathered = jnp.dot(extended, select_mat.T, precision=highest)
    local = jnp.dot(far_trans, gathered, precision=highest)
    spread = jnp.dot(local, slot_table, precision=highest)
    return self_diag[None, :] * field + jnp.dot(self_trans, field, precision=highest) + spread


def least_squares(hessen, beta_norm):
    (h00, h01), (h10, h11), (h20, h21) = hessen
    g00 = h00 * h00 + h10 * h10 + h20 * h20
    g01 = h00 * h01 + h10 * h11 + h20 * h21
    g11 = h01 * h01 + h11 * h11 + h21 * h21
    l00 = jnp.sqrt(g00)
    l10 = g01 / l00
    l11 = jnp.sqrt(g11 - l10 * l10)
    f0 = beta_norm * h00 / l00
    f1 = (beta_norm * h01 - l10 * f0) / l11
    y1 = f1 / l11
    y0 = (f0 - l10 * y1) / l00
    return y0, y1


def on_device(right_side, group_ids, pair_sources, pair_weights, self_diag, self_trans, far_trans):
    group_count = pair_sources.shape[0]
    base_group = lax.axis_index(DEVICES) * group_count
    slots = group_ids - base_group
    slot_table = (slots[None, :] == jnp.arange(group_count, dtype=jnp.int32)[:, None]).astype(
        jnp.float32
    )
    columns = base_group - group_count + jnp.arange(3 * group_count, dtype=jnp.int32)
    matches = (pair_sources[:, :, None] == columns[None, None, :]).astype(jnp.float32)
    select_mat = jnp.sum(pair_weights[:, :, None] * matches, axis=1)
    operator = lambda field: apply_operator(
        field, slot_table, select_mat, self_diag, self_trans, far_trans
    )
    first = operator(right_side)
    second = operator(first)
    krylov = (right_side, first, second)
    partials = jnp.stack([jnp.sum(krylov[i] * krylov[j]) for i, j in GRAM_PAIRS])
    totals = lax.psum(partials, DEVICES)
    g00, g01, g02, g11, g12, g22 = [totals[k] for k in range(6)]
    beta_norm = jnp.sqrt(g00)
    h00 = g01 / g00
    h10 = jnp.sqrt(g11 / g00 - h00 * h00)
    scale = beta_norm * h10
    h01 = (g02 - h00 * g01) / (beta_norm * scale)
    h11 = (g12 - h00 * g11 - h00 * g02 + h00 * h00 * g01) / (scale * scale)
    ww1 = (g22 - 2.0 * h00 * g12 + h00 * h00 * g11) / (scale * scale)
    h21 = jnp.sqrt(ww1 - h01 * h01 - h11 * h11)
    zero = jnp.zeros((), jnp.float32)
    y0, y1 = least_squares(((h00, h01), (h10, h11), (zero, h21)), beta_norm)
    c1 = y1 / scale
    c0 = y0 / beta_norm - c1 * h00
    return c0 * right_side + c1 * first


def solution(mesh):
    placed = (
        P(None, DEVICES),
        P(DEVICES),
        P(DEVICES, None),
        P(DEVICES, None),
        P(DEVICES),
        P(),
        P(),
    )
    return jax.shard_map(
        on_device, mesh=mesh, in_specs=placed, out_specs=P(None, DEVICES), check_vma=False
    )
```

```python
import jax
import jax.numpy as jnp
from jax import lax
from jax.sharding import PartitionSpec as P

ITERS = 2
DEVICES = ("curve", "coef")
GRAM_PAIRS = ((0, 0), (0, 1), (0, 2), (1, 1), (1, 2), (2, 2))


def shifted(array, axis, by):
    peers = lax.axis_size(axis)
    pairs = [(i, i + by) for i in range(peers) if 0 <= i + by < peers]
    return lax.ppermute(array, axis, pairs)


def all_sum(value):
    peers = lax.axis_size(DEVICES)
    rounds = peers.bit_length() - 1
    for bit in range(rounds):
        pairs = [(i, i ^ (1 << bit)) for i in range(peers)]
        value = value + lax.ppermute(value, DEVICES, pairs)
    return value


def apply_operator(field, slot_table, select_mat, self_diag, self_trans, far_trans):
    highest = lax.Precision.HIGHEST
    moments = jnp.dot(field, slot_table.T, precision=highest)
    lower = shifted(moments, DEVICES, 1)
    upper = shifted(moments, DEVICES, -1)
    extended = jnp.concatenate([lower, moments, upper], axis=1)
    gathered = jnp.dot(extended, select_mat.T, precision=highest)
    local = jnp.dot(far_trans, gathered, precision=highest)
    spread = jnp.dot(local, slot_table, precision=highest)
    return self_diag[None, :] * field + jnp.dot(self_trans, field, precision=highest) + spread


def least_squares(hessen, beta_norm):
    (h00, h01), (h10, h11), (h20, h21) = hessen
    g00 = h00 * h00 + h10 * h10 + h20 * h20
    g01 = h00 * h01 + h10 * h11 + h20 * h21
    g11 = h01 * h01 + h11 * h11 + h21 * h21
    l00 = jnp.sqrt(g00)
    l10 = g01 / l00
    l11 = jnp.sqrt(g11 - l10 * l10)
    f0 = beta_norm * h00 / l00
    f1 = (beta_norm * h01 - l10 * f0) / l11
    y1 = f1 / l11
    y0 = (f0 - l10 * y1) / l00
    return y0, y1


def on_device(right_side, group_ids, pair_sources, pair_weights, self_diag, self_trans, far_trans):
    group_count = pair_sources.shape[0]
    base_group = lax.axis_index(DEVICES) * group_count
    slots = group_ids - base_group
    slot_table = (slots[None, :] == jnp.arange(group_count, dtype=jnp.int32)[:, None]).astype(
        jnp.float32
    )
    columns = base_group - group_count + jnp.arange(3 * group_count, dtype=jnp.int32)
    matches = (pair_sources[:, :, None] == columns[None, None, :]).astype(jnp.float32)
    select_mat = jnp.sum(pair_weights[:, :, None] * matches, axis=1)
    operator = lambda field: apply_operator(
        field, slot_table, select_mat, self_diag, self_trans, far_trans
    )
    first = operator(right_side)
    second = operator(first)
    krylov = (right_side, first, second)
    columns_sums = jnp.stack([jnp.sum(krylov[i] * krylov[j], axis=0) for i, j in GRAM_PAIRS])
    partials = jnp.sum(columns_sums, axis=1)
    totals = all_sum(partials)
    lanes = lax.optimization_barrier(jnp.broadcast_to(totals[:, None], (len(GRAM_PAIRS), 128)))
    g00, g01, g02, g11, g12, g22 = [lanes[k] for k in range(len(GRAM_PAIRS))]
    beta_norm = jnp.sqrt(g00)
    h00 = g01 / g00
    h10 = jnp.sqrt(g11 / g00 - h00 * h00)
    scale = beta_norm * h10
    h01 = (g02 - h00 * g01) / (beta_norm * scale)
    h11 = (g12 - h00 * g11 - h00 * g02 + h00 * h00 * g01) / (scale * scale)
    ww1 = (g22 - 2.0 * h00 * g12 + h00 * h00 * g11) / (scale * scale)
    h21 = jnp.sqrt(ww1 - h01 * h01 - h11 * h11)
    zero = jnp.zeros_like(h00)
    y0, y1 = least_squares(((h00, h01), (h10, h11), (zero, h21)), beta_norm)
    c1 = y1 / scale
    c0 = y0 / beta_norm - c1 * h00
    c0, c1 = lax.optimization_barrier((c0, c1))
    return c0[0] * right_side + c1[0] * first


def solution(mesh):
    placed = (
        P(None, DEVICES),
        P(DEVICES),
        P(DEVICES, None),
        P(DEVICES, None),
        P(DEVICES),
        P(),
        P(),
    )
    return jax.shard_map(
        on_device, mesh=mesh, in_specs=placed, out_specs=P(None, DEVICES), check_vma=False
    )
```

```python
import jax
import jax.numpy as jnp
from jax import lax
from jax.sharding import PartitionSpec as P

ITERS = 2
DEVICES = ("curve", "coef")
GRAM_PAIRS = ((0, 0), (0, 1), (0, 2), (1, 1), (1, 2), (2, 2))


def shifted(array, axis, by):
    peers = lax.axis_size(axis)
    pairs = [(i, i + by) for i in range(peers) if 0 <= i + by < peers]
    return lax.ppermute(array, axis, pairs)


def all_sum(value):
    for axis in ("coef", "curve"):
        peers = lax.axis_size(axis)
        spread = jnp.broadcast_to(value[None, :], (peers,) + value.shape)
        value = jnp.sum(lax.all_to_all(spread, axis, 0, 0, tiled=True), axis=0)
    return value


def apply_operator(field, slot_table, select_mat, self_diag, self_trans, far_trans):
    highest = lax.Precision.HIGHEST
    moments = jnp.dot(field, slot_table.T, precision=highest)
    lower = shifted(moments, DEVICES, 1)
    upper = shifted(moments, DEVICES, -1)
    extended = jnp.concatenate([lower, moments, upper], axis=1)
    gathered = jnp.dot(extended, select_mat.T, precision=highest)
    local = jnp.dot(far_trans, gathered, precision=highest)
    spread = jnp.dot(local, slot_table, precision=highest)
    return self_diag[None, :] * field + jnp.dot(self_trans, field, precision=highest) + spread


def least_squares(hessen, beta_norm):
    (h00, h01), (h10, h11), (h20, h21) = hessen
    g00 = h00 * h00 + h10 * h10 + h20 * h20
    g01 = h00 * h01 + h10 * h11 + h20 * h21
    g11 = h01 * h01 + h11 * h11 + h21 * h21
    l00 = jnp.sqrt(g00)
    l10 = g01 / l00
    l11 = jnp.sqrt(g11 - l10 * l10)
    f0 = beta_norm * h00 / l00
    f1 = (beta_norm * h01 - l10 * f0) / l11
    y1 = f1 / l11
    y0 = (f0 - l10 * y1) / l00
    return y0, y1


def on_device(right_side, group_ids, pair_sources, pair_weights, self_diag, self_trans, far_trans):
    group_count = pair_sources.shape[0]
    base_group = lax.axis_index(DEVICES) * group_count
    slots = group_ids - base_group
    slot_table = (slots[None, :] == jnp.arange(group_count, dtype=jnp.int32)[:, None]).astype(
        jnp.float32
    )
    columns = base_group - group_count + jnp.arange(3 * group_count, dtype=jnp.int32)
    matches = (pair_sources[:, :, None] == columns[None, None, :]).astype(jnp.float32)
    select_mat = jnp.sum(pair_weights[:, :, None] * matches, axis=1)
    operator = lambda field: apply_operator(
        field, slot_table, select_mat, self_diag, self_trans, far_trans
    )
    first = operator(right_side)
    second = operator(first)
    krylov = (right_side, first, second)
    columns_sums = jnp.stack([jnp.sum(krylov[i] * krylov[j], axis=0) for i, j in GRAM_PAIRS])
    partials = jnp.sum(columns_sums, axis=1)
    totals = all_sum(partials)
    lanes = lax.optimization_barrier(jnp.broadcast_to(totals[:, None], (len(GRAM_PAIRS), 128)))
    g00, g01, g02, g11, g12, g22 = [lanes[k] for k in range(len(GRAM_PAIRS))]
    beta_norm = jnp.sqrt(g00)
    h00 = g01 / g00
    h10 = jnp.sqrt(g11 / g00 - h00 * h00)
    scale = beta_norm * h10
    h01 = (g02 - h00 * g01) / (beta_norm * scale)
    h11 = (g12 - h00 * g11 - h00 * g02 + h00 * h00 * g01) / (scale * scale)
    ww1 = (g22 - 2.0 * h00 * g12 + h00 * h00 * g11) / (scale * scale)
    h21 = jnp.sqrt(ww1 - h01 * h01 - h11 * h11)
    zero = jnp.zeros_like(h00)
    y0, y1 = least_squares(((h00, h01), (h10, h11), (zero, h21)), beta_norm)
    c1 = y1 / scale
    c0 = y0 / beta_norm - c1 * h00
    c0, c1 = lax.optimization_barrier((c0, c1))
    return c0[0] * right_side + c1[0] * first


def solution(mesh):
    placed = (
        P(None, DEVICES),
        P(DEVICES),
        P(DEVICES, None),
        P(DEVICES, None),
        P(DEVICES),
        P(),
        P(),
    )
    return jax.shard_map(
        on_device, mesh=mesh, in_specs=placed, out_specs=P(None, DEVICES), check_vma=False
    )
```

```python
import jax
import jax.numpy as jnp
from jax import lax
from jax.sharding import PartitionSpec as P

ITERS = 2
DEVICES = ("curve", "coef")
GRAM_PAIRS = ((0, 0), (0, 1), (0, 2), (1, 1), (1, 2), (2, 2))


def shifted(array, axis, by):
    peers = lax.axis_size(axis)
    pairs = [(i, i + by) for i in range(peers) if 0 <= i + by < peers]
    return lax.ppermute(array, axis, pairs)


def all_sum(value):
    for axis in ("coef", "curve"):
        peers = lax.axis_size(axis)
        spread = jnp.broadcast_to(value[None, :], (peers,) + value.shape)
        value = jnp.sum(lax.all_to_all(spread, axis, 0, 0, tiled=True), axis=0)
    return value


def local_part(field, self_diag, self_trans):
    highest = lax.Precision.HIGHEST
    return self_diag[None, :] * field + jnp.dot(self_trans, field, precision=highest)


def least_squares(hessen, beta_norm):
    (h00, h01), (h10, h11), (h20, h21) = hessen
    g00 = h00 * h00 + h10 * h10 + h20 * h20
    g01 = h00 * h01 + h10 * h11 + h20 * h21
    g11 = h01 * h01 + h11 * h11 + h21 * h21
    l00 = jnp.sqrt(g00)
    l10 = g01 / l00
    l11 = jnp.sqrt(g11 - l10 * l10)
    f0 = beta_norm * h00 / l00
    f1 = (beta_norm * h01 - l10 * f0) / l11
    y1 = f1 / l11
    y0 = (f0 - l10 * y1) / l00
    return y0, y1


def on_device(right_side, group_ids, pair_sources, pair_weights, self_diag, self_trans, far_trans):
    group_count = pair_sources.shape[0]
    base_group = lax.axis_index(DEVICES) * group_count
    slots = group_ids - base_group
    slot_table = (slots[None, :] == jnp.arange(group_count, dtype=jnp.int32)[:, None]).astype(
        jnp.float32
    )
    columns = base_group - group_count + jnp.arange(3 * group_count, dtype=jnp.int32)
    matches = (pair_sources[:, :, None] == columns[None, None, :]).astype(jnp.float32)
    select_mat = jnp.sum(pair_weights[:, :, None] * matches, axis=1)
    counts = jnp.sum(slot_table, axis=1)
    highest = lax.Precision.HIGHEST
    dot = lambda a, b: jnp.dot(a, b, precision=highest)
    moments = dot(right_side, slot_table.T)
    own_part = dot(right_side * self_diag[None, :], slot_table.T) + dot(self_trans, moments)
    g = group_count
    filler = jnp.zeros((g, g), jnp.float32)
    payload = jnp.concatenate(
        [
            jnp.concatenate([moments, own_part, jnp.zeros_like(moments)], axis=1),
            select_mat,
            jnp.concatenate([counts[:, None], jnp.zeros((g, 3 * g - 1), jnp.float32)], axis=1),
        ],
        axis=0,
    )
    rows = moments.shape[0]
    below = shifted(payload, DEVICES, 1)
    above = shifted(payload, DEVICES, -1)
    two_below = shifted(moments, DEVICES, 2)
    two_above = shifted(moments, DEVICES, -2)
    unpack = lambda block: (
        block[:rows, :g],
        block[:rows, g : 2 * g],
        block[rows : rows + g],
        block[rows + g :, 0],
    )
    moments_below, part_below, select_below, counts_below = unpack(below)
    moments_above, part_above, select_above, counts_above = unpack(above)
    wide = jnp.concatenate([two_below, moments_below, moments, moments_above, two_above], axis=1)
    wide_select = jnp.concatenate(
        [
            jnp.concatenate([select_below, filler, filler], axis=1),
            jnp.concatenate([filler, select_mat, filler], axis=1),
            jnp.concatenate([filler, filler, select_above], axis=1),
        ],
        axis=0,
    )
    local_near = dot(far_trans, dot(wide, wide_select.T))
    near_counts = jnp.concatenate([counts_below, counts, counts_above])
    near_part = jnp.concatenate([part_below, own_part, part_above], axis=1)
    near_moments = near_part + near_counts[None, :] * local_near
    first = local_part(right_side, self_diag, self_trans) + dot(local_near[:, g : 2 * g], slot_table)
    local_next = dot(far_trans, dot(near_moments, select_mat.T))
    second = local_part(first, self_diag, self_trans) + dot(local_next, slot_table)
    krylov = (right_side, first, second)
    columns_sums = jnp.stack([jnp.sum(krylov[i] * krylov[j], axis=0) for i, j in GRAM_PAIRS])
    partials = jnp.sum(columns_sums, axis=1)
    totals = all_sum(partials)
    lanes = lax.optimization_barrier(jnp.broadcast_to(totals[:, None], (len(GRAM_PAIRS), 128)))
    g00, g01, g02, g11, g12, g22 = [lanes[k] for k in range(len(GRAM_PAIRS))]
    beta_norm = jnp.sqrt(g00)
    h00 = g01 / g00
    h10 = jnp.sqrt(g11 / g00 - h00 * h00)
    scale = beta_norm * h10
    h01 = (g02 - h00 * g01) / (beta_norm * scale)
    h11 = (g12 - h00 * g11 - h00 * g02 + h00 * h00 * g01) / (scale * scale)
    ww1 = (g22 - 2.0 * h00 * g12 + h00 * h00 * g11) / (scale * scale)
    h21 = jnp.sqrt(ww1 - h01 * h01 - h11 * h11)
    zero = jnp.zeros_like(h00)
    y0, y1 = least_squares(((h00, h01), (h10, h11), (zero, h21)), beta_norm)
    c1 = y1 / scale
    c0 = y0 / beta_norm - c1 * h00
    c0, c1 = lax.optimization_barrier((c0, c1))
    return c0[0] * right_side + c1[0] * first


def solution(mesh):
    placed = (
        P(None, DEVICES),
        P(DEVICES),
        P(DEVICES, None),
        P(DEVICES, None),
        P(DEVICES),
        P(),
        P(),
    )
    return jax.shard_map(
        on_device, mesh=mesh, in_specs=placed, out_specs=P(None, DEVICES), check_vma=False
    )
```

```python
import jax
import jax.numpy as jnp
from jax import lax
from jax.sharding import PartitionSpec as P

ITERS = 2
DEVICES = ("curve", "coef")
GRAM_PAIRS = ((0, 0), (0, 1), (0, 2), (1, 1), (1, 2), (2, 2))


def shifted(array, axis, by):
    peers = lax.axis_size(axis)
    pairs = [(i, i + by) for i in range(peers) if 0 <= i + by < peers]
    return lax.ppermute(array, axis, pairs)


def all_sum(value):
    for axis in ("coef", "curve"):
        peers = lax.axis_size(axis)
        spread = jnp.broadcast_to(value[None, :], (peers,) + value.shape)
        value = jnp.sum(lax.all_to_all(spread, axis, 0, 0, tiled=True), axis=0)
    return value


def local_part(field, self_diag, self_trans):
    highest = lax.Precision.HIGHEST
    return self_diag[None, :] * field + jnp.dot(self_trans, field, precision=highest)


def least_squares(hessen, beta_norm):
    (h00, h01), (h10, h11), (h20, h21) = hessen
    g00 = h00 * h00 + h10 * h10 + h20 * h20
    g01 = h00 * h01 + h10 * h11 + h20 * h21
    g11 = h01 * h01 + h11 * h11 + h21 * h21
    l00 = jnp.sqrt(g00)
    l10 = g01 / l00
    l11 = jnp.sqrt(g11 - l10 * l10)
    f0 = beta_norm * h00 / l00
    f1 = (beta_norm * h01 - l10 * f0) / l11
    y1 = f1 / l11
    y0 = (f0 - l10 * y1) / l00
    return y0, y1


def on_device(right_side, group_ids, pair_sources, pair_weights, self_diag, self_trans, far_trans):
    group_count = pair_sources.shape[0]
    base_group = lax.axis_index(DEVICES) * group_count
    slots = group_ids - base_group
    slot_table = (slots[None, :] == jnp.arange(group_count, dtype=jnp.int32)[:, None]).astype(
        jnp.float32
    )
    columns = base_group - group_count + jnp.arange(3 * group_count, dtype=jnp.int32)
    matches = (pair_sources[:, :, None] == columns[None, None, :]).astype(jnp.float32)
    select_mat = jnp.sum(pair_weights[:, :, None] * matches, axis=1)
    counts = jnp.sum(slot_table, axis=1)
    highest = lax.Precision.HIGHEST
    dot = lambda a, b: jnp.dot(a, b, precision=highest)
    moments = dot(right_side, slot_table.T)
    own_part = dot(right_side * self_diag[None, :], slot_table.T) + dot(self_trans, moments)
    g = group_count
    filler = jnp.zeros((g, g), jnp.float32)
    payload = jnp.concatenate(
        [
            jnp.concatenate([moments, own_part, jnp.zeros_like(moments)], axis=1),
            select_mat,
            jnp.concatenate([counts[:, None], jnp.zeros((g, 3 * g - 1), jnp.float32)], axis=1),
        ],
        axis=0,
    )
    rows = moments.shape[0]
    payload, moments = lax.optimization_barrier((payload, moments))
    below = shifted(payload, DEVICES, 1)
    above = shifted(payload, DEVICES, -1)
    two_below = shifted(moments, DEVICES, 2)
    two_above = shifted(moments, DEVICES, -2)
    unpack = lambda block: (
        block[:rows, :g],
        block[:rows, g : 2 * g],
        block[rows : rows + g],
        block[rows + g :, 0],
    )
    moments_below, part_below, select_below, counts_below = unpack(below)
    moments_above, part_above, select_above, counts_above = unpack(above)
    wide = jnp.concatenate([two_below, moments_below, moments, moments_above, two_above], axis=1)
    wide_select = jnp.concatenate(
        [
            jnp.concatenate([select_below, filler, filler], axis=1),
            jnp.concatenate([filler, select_mat, filler], axis=1),
            jnp.concatenate([filler, filler, select_above], axis=1),
        ],
        axis=0,
    )
    local_near = dot(far_trans, dot(wide, wide_select.T))
    near_counts = jnp.concatenate([counts_below, counts, counts_above])
    near_part = jnp.concatenate([part_below, own_part, part_above], axis=1)
    near_moments = near_part + near_counts[None, :] * local_near
    first = local_part(right_side, self_diag, self_trans) + dot(local_near[:, g : 2 * g], slot_table)
    local_next = dot(far_trans, dot(near_moments, select_mat.T))
    second = local_part(first, self_diag, self_trans) + dot(local_next, slot_table)
    krylov = (right_side, first, second)
    columns_sums = jnp.stack([jnp.sum(krylov[i] * krylov[j], axis=0) for i, j in GRAM_PAIRS])
    partials = jnp.sum(columns_sums, axis=1)
    totals = all_sum(partials)
    lanes = lax.optimization_barrier(jnp.broadcast_to(totals[:, None], (len(GRAM_PAIRS), 128)))
    g00, g01, g02, g11, g12, g22 = [lanes[k] for k in range(len(GRAM_PAIRS))]
    beta_norm = jnp.sqrt(g00)
    h00 = g01 / g00
    h10 = jnp.sqrt(g11 / g00 - h00 * h00)
    scale = beta_norm * h10
    h01 = (g02 - h00 * g01) / (beta_norm * scale)
    h11 = (g12 - h00 * g11 - h00 * g02 + h00 * h00 * g01) / (scale * scale)
    ww1 = (g22 - 2.0 * h00 * g12 + h00 * h00 * g11) / (scale * scale)
    h21 = jnp.sqrt(ww1 - h01 * h01 - h11 * h11)
    zero = jnp.zeros_like(h00)
    y0, y1 = least_squares(((h00, h01), (h10, h11), (zero, h21)), beta_norm)
    c1 = y1 / scale
    c0 = y0 / beta_norm - c1 * h00
    c0, c1 = lax.optimization_barrier((c0, c1))
    return c0[0] * right_side + c1[0] * first


def solution(mesh):
    placed = (
        P(None, DEVICES),
        P(DEVICES),
        P(DEVICES, None),
        P(DEVICES, None),
        P(DEVICES),
        P(),
        P(),
    )
    return jax.shard_map(
        on_device, mesh=mesh, in_specs=placed, out_specs=P(None, DEVICES), check_vma=False
    )
```

```python
import jax
import jax.numpy as jnp
from jax import lax
from jax.sharding import PartitionSpec as P

ITERS = 2
DEVICES = ("curve", "coef")
GRAM_PAIRS = ((0, 0), (0, 1), (0, 2), (1, 1), (1, 2), (2, 2))


def shifted(array, axis, by):
    peers = lax.axis_size(axis)
    pairs = [(i, i + by) for i in range(peers) if 0 <= i + by < peers]
    return lax.ppermute(array, axis, pairs)


def all_sum(value):
    for axis in ("coef", "curve"):
        peers = lax.axis_size(axis)
        spread = jnp.broadcast_to(value[None, :], (peers,) + value.shape)
        value = jnp.sum(lax.all_to_all(spread, axis, 0, 0, tiled=True), axis=0)
    return value


def local_part(field, self_diag, self_trans):
    highest = lax.Precision.HIGHEST
    return self_diag[None, :] * field + jnp.dot(self_trans, field, precision=highest)


def least_squares(hessen, beta_norm):
    (h00, h01), (h10, h11), (h20, h21) = hessen
    g00 = h00 * h00 + h10 * h10 + h20 * h20
    g01 = h00 * h01 + h10 * h11 + h20 * h21
    g11 = h01 * h01 + h11 * h11 + h21 * h21
    l00 = jnp.sqrt(g00)
    l10 = g01 / l00
    l11 = jnp.sqrt(g11 - l10 * l10)
    f0 = beta_norm * h00 / l00
    f1 = (beta_norm * h01 - l10 * f0) / l11
    y1 = f1 / l11
    y0 = (f0 - l10 * y1) / l00
    return y0, y1


def on_device(right_side, group_ids, pair_sources, pair_weights, self_diag, self_trans, far_trans):
    group_count = pair_sources.shape[0]
    base_group = lax.axis_index(DEVICES) * group_count
    slots = group_ids - base_group
    slot_table = (slots[None, :] == jnp.arange(group_count, dtype=jnp.int32)[:, None]).astype(
        jnp.float32
    )
    columns = base_group - group_count + jnp.arange(3 * group_count, dtype=jnp.int32)
    matches = (pair_sources[:, :, None] == columns[None, None, :]).astype(jnp.float32)
    select_mat = jnp.sum(pair_weights[:, :, None] * matches, axis=1)
    counts = jnp.sum(slot_table, axis=1)
    highest = lax.Precision.HIGHEST
    dot = lambda a, b: jnp.dot(a, b, precision=highest)
    moments = dot(right_side, slot_table.T)
    own_part = dot(right_side * self_diag[None, :], slot_table.T) + dot(self_trans, moments)
    moments = dot(far_trans, moments)
    g = group_count
    filler = jnp.zeros((g, g), jnp.float32)
    payload = jnp.concatenate(
        [
            jnp.concatenate([moments, own_part, jnp.zeros_like(moments)], axis=1),
            select_mat,
            jnp.concatenate([counts[:, None], jnp.zeros((g, 3 * g - 1), jnp.float32)], axis=1),
        ],
        axis=0,
    )
    rows = moments.shape[0]
    payload, moments = lax.optimization_barrier((payload, moments))
    below = shifted(payload, DEVICES, 1)
    above = shifted(payload, DEVICES, -1)
    two_below = shifted(moments, DEVICES, 2)
    two_above = shifted(moments, DEVICES, -2)
    unpack = lambda block: (
        block[:rows, :g],
        block[:rows, g : 2 * g],
        block[rows : rows + g],
        block[rows + g :, 0],
    )
    moments_below, part_below, select_below, counts_below = unpack(below)
    moments_above, part_above, select_above, counts_above = unpack(above)
    wide = jnp.concatenate([two_below, moments_below, moments, moments_above, two_above], axis=1)
    wide_select = jnp.concatenate(
        [
            jnp.concatenate([select_below, filler, filler], axis=1),
            jnp.concatenate([filler, select_mat, filler], axis=1),
            jnp.concatenate([filler, filler, select_above], axis=1),
        ],
        axis=0,
    )
    local_near = dot(wide, wide_select.T)
    near_counts = jnp.concatenate([counts_below, counts, counts_above])
    near_part = jnp.concatenate([part_below, own_part, part_above], axis=1)
    near_moments = near_part + near_counts[None, :] * local_near
    first = local_part(right_side, self_diag, self_trans) + dot(local_near[:, g : 2 * g], slot_table)
    local_next = dot(far_trans, dot(near_moments, select_mat.T))
    second = local_part(first, self_diag, self_trans) + dot(local_next, slot_table)
    krylov = (right_side, first, second)
    columns_sums = jnp.stack([jnp.sum(krylov[i] * krylov[j], axis=0) for i, j in GRAM_PAIRS])
    partials = jnp.sum(columns_sums, axis=1)
    totals = all_sum(partials)
    lanes = lax.optimization_barrier(jnp.broadcast_to(totals[:, None], (len(GRAM_PAIRS), 128)))
    g00, g01, g02, g11, g12, g22 = [lanes[k] for k in range(len(GRAM_PAIRS))]
    beta_norm = jnp.sqrt(g00)
    h00 = g01 / g00
    h10 = jnp.sqrt(g11 / g00 - h00 * h00)
    scale = beta_norm * h10
    h01 = (g02 - h00 * g01) / (beta_norm * scale)
    h11 = (g12 - h00 * g11 - h00 * g02 + h00 * h00 * g01) / (scale * scale)
    ww1 = (g22 - 2.0 * h00 * g12 + h00 * h00 * g11) / (scale * scale)
    h21 = jnp.sqrt(ww1 - h01 * h01 - h11 * h11)
    zero = jnp.zeros_like(h00)
    y0, y1 = least_squares(((h00, h01), (h10, h11), (zero, h21)), beta_norm)
    c1 = y1 / scale
    c0 = y0 / beta_norm - c1 * h00
    c0, c1 = lax.optimization_barrier((c0, c1))
    return c0[0] * right_side + c1[0] * first


def solution(mesh):
    placed = (
        P(None, DEVICES),
        P(DEVICES),
        P(DEVICES, None),
        P(DEVICES, None),
        P(DEVICES),
        P(),
        P(),
    )
    return jax.shard_map(
        on_device, mesh=mesh, in_specs=placed, out_specs=P(None, DEVICES), check_vma=False
    )
```

```python
import jax
import jax.numpy as jnp
from jax import lax
from jax.sharding import PartitionSpec as P

ITERS = 2
DEVICES = ("curve", "coef")
GRAM_PAIRS = ((0, 0), (0, 1), (0, 2), (1, 1), (1, 2), (2, 2))


def shifted(array, axis, by):
    peers = lax.axis_size(axis)
    pairs = [(i, i + by) for i in range(peers) if 0 <= i + by < peers]
    return lax.ppermute(array, axis, pairs)


def all_sum(value):
    for axis in ("coef", "curve"):
        peers = lax.axis_size(axis)
        spread = jnp.broadcast_to(value[None, :], (peers,) + value.shape)
        value = jnp.sum(lax.all_to_all(spread, axis, 0, 0, tiled=True), axis=0)
    return value


def local_part(field, self_diag, self_trans):
    highest = lax.Precision.HIGHEST
    return self_diag[None, :] * field + jnp.dot(self_trans, field, precision=highest)


def least_squares(hessen, beta_norm):
    (h00, h01), (h10, h11), (h20, h21) = hessen
    g00 = h00 * h00 + h10 * h10 + h20 * h20
    g01 = h00 * h01 + h10 * h11 + h20 * h21
    g11 = h01 * h01 + h11 * h11 + h21 * h21
    l00 = jnp.sqrt(g00)
    l10 = g01 / l00
    l11 = jnp.sqrt(g11 - l10 * l10)
    f0 = beta_norm * h00 / l00
    f1 = (beta_norm * h01 - l10 * f0) / l11
    y1 = f1 / l11
    y0 = (f0 - l10 * y1) / l00
    return y0, y1


def on_device(right_side, group_ids, pair_sources, pair_weights, self_diag, self_trans, far_trans):
    group_count = pair_sources.shape[0]
    base_group = lax.axis_index(DEVICES) * group_count
    slots = group_ids - base_group
    slot_table = (slots[None, :] == jnp.arange(group_count, dtype=jnp.int32)[:, None]).astype(
        jnp.float32
    )
    columns = base_group - group_count + jnp.arange(3 * group_count, dtype=jnp.int32)
    matches = (pair_sources[:, :, None] == columns[None, None, :]).astype(jnp.float32)
    select_mat = jnp.sum(pair_weights[:, :, None] * matches, axis=1)
    counts = jnp.sum(slot_table, axis=1)
    highest = lax.Precision.HIGHEST
    dot = lambda a, b: jnp.dot(a, b, precision=highest)
    onehot_right = lambda a, b: jnp.dot(a, b, precision=(highest, lax.Precision.DEFAULT))
    moments = onehot_right(right_side, slot_table.T)
    own_part = onehot_right(right_side * self_diag[None, :], slot_table.T) + dot(self_trans, moments)
    moments = dot(far_trans, moments)
    g = group_count
    filler = jnp.zeros((g, g), jnp.float32)
    payload = jnp.concatenate(
        [
            jnp.concatenate([moments, own_part, jnp.zeros_like(moments)], axis=1),
            select_mat,
            jnp.concatenate([counts[:, None], jnp.zeros((g, 3 * g - 1), jnp.float32)], axis=1),
        ],
        axis=0,
    )
    rows = moments.shape[0]
    payload, moments = lax.optimization_barrier((payload, moments))
    below = shifted(payload, DEVICES, 1)
    above = shifted(payload, DEVICES, -1)
    two_below = shifted(moments, DEVICES, 2)
    two_above = shifted(moments, DEVICES, -2)
    unpack = lambda block: (
        block[:rows, :g],
        block[:rows, g : 2 * g],
        block[rows : rows + g],
        block[rows + g :, 0],
    )
    moments_below, part_below, select_below, counts_below = unpack(below)
    moments_above, part_above, select_above, counts_above = unpack(above)
    wide = jnp.concatenate([two_below, moments_below, moments, moments_above, two_above], axis=1)
    wide_select = jnp.concatenate(
        [
            jnp.concatenate([select_below, filler, filler], axis=1),
            jnp.concatenate([filler, select_mat, filler], axis=1),
            jnp.concatenate([filler, filler, select_above], axis=1),
        ],
        axis=0,
    )
    local_near = dot(wide, wide_select.T)
    near_counts = jnp.concatenate([counts_below, counts, counts_above])
    near_part = jnp.concatenate([part_below, own_part, part_above], axis=1)
    near_moments = near_part + near_counts[None, :] * local_near
    first = local_part(right_side, self_diag, self_trans) + onehot_right(local_near[:, g : 2 * g], slot_table)
    local_next = dot(far_trans, dot(near_moments, select_mat.T))
    second = local_part(first, self_diag, self_trans) + onehot_right(local_next, slot_table)
    krylov = (right_side, first, second)
    columns_sums = jnp.stack([jnp.sum(krylov[i] * krylov[j], axis=0) for i, j in GRAM_PAIRS])
    partials = jnp.sum(columns_sums, axis=1)
    totals = all_sum(partials)
    lanes = lax.optimization_barrier(jnp.broadcast_to(totals[:, None], (len(GRAM_PAIRS), 128)))
    g00, g01, g02, g11, g12, g22 = [lanes[k] for k in range(len(GRAM_PAIRS))]
    beta_norm = jnp.sqrt(g00)
    h00 = g01 / g00
    h10 = jnp.sqrt(g11 / g00 - h00 * h00)
    scale = beta_norm * h10
    h01 = (g02 - h00 * g01) / (beta_norm * scale)
    h11 = (g12 - h00 * g11 - h00 * g02 + h00 * h00 * g01) / (scale * scale)
    ww1 = (g22 - 2.0 * h00 * g12 + h00 * h00 * g11) / (scale * scale)
    h21 = jnp.sqrt(ww1 - h01 * h01 - h11 * h11)
    zero = jnp.zeros_like(h00)
    y0, y1 = least_squares(((h00, h01), (h10, h11), (zero, h21)), beta_norm)
    c1 = y1 / scale
    c0 = y0 / beta_norm - c1 * h00
    c0, c1 = lax.optimization_barrier((c0, c1))
    return c0[0] * right_side + c1[0] * first


def solution(mesh):
    placed = (
        P(None, DEVICES),
        P(DEVICES),
        P(DEVICES, None),
        P(DEVICES, None),
        P(DEVICES),
        P(),
        P(),
    )
    return jax.shard_map(
        on_device, mesh=mesh, in_specs=placed, out_specs=P(None, DEVICES), check_vma=False
    )
```

```python
import jax
import jax.numpy as jnp
from jax import lax
from jax.sharding import PartitionSpec as P

ITERS = 2
DEVICES = ("curve", "coef")
GRAM_PAIRS = ((0, 0), (0, 1), (0, 2), (1, 1), (1, 2), (2, 2))


def shifted(array, axis, by):
    peers = lax.axis_size(axis)
    pairs = [(i, i + by) for i in range(peers) if 0 <= i + by < peers]
    return lax.ppermute(array, axis, pairs)


def all_sum(value):
    for axis in ("coef", "curve"):
        peers = lax.axis_size(axis)
        spread = jnp.broadcast_to(value[None, :], (peers,) + value.shape)
        value = jnp.sum(lax.all_to_all(spread, axis, 0, 0, tiled=True), axis=0)
    return value


def local_part(field, self_diag, self_trans):
    highest = lax.Precision.HIGHEST
    return self_diag[None, :] * field + jnp.dot(self_trans, field, precision=highest)


def least_squares(hessen, beta_norm):
    (h00, h01), (h10, h11), (h20, h21) = hessen
    g00 = h00 * h00 + h10 * h10 + h20 * h20
    g01 = h00 * h01 + h10 * h11 + h20 * h21
    g11 = h01 * h01 + h11 * h11 + h21 * h21
    l00 = jnp.sqrt(g00)
    l10 = g01 / l00
    l11 = jnp.sqrt(g11 - l10 * l10)
    f0 = beta_norm * h00 / l00
    f1 = (beta_norm * h01 - l10 * f0) / l11
    y1 = f1 / l11
    y0 = (f0 - l10 * y1) / l00
    return y0, y1


def on_device(right_side, group_ids, pair_sources, pair_weights, self_diag, self_trans, far_trans):
    group_count = pair_sources.shape[0]
    base_group = lax.axis_index(DEVICES) * group_count
    slots = group_ids - base_group
    slot_table = (slots[None, :] == jnp.arange(group_count, dtype=jnp.int32)[:, None]).astype(
        jnp.float32
    )
    columns = base_group - group_count + jnp.arange(3 * group_count, dtype=jnp.int32)
    matches = (pair_sources[:, :, None] == columns[None, None, :]).astype(jnp.float32)
    select_mat = jnp.sum(pair_weights[:, :, None] * matches, axis=1)
    counts = jnp.sum(slot_table, axis=1)
    highest = lax.Precision.HIGHEST
    dot = lambda a, b: jnp.dot(a, b, precision=highest)
    onehot_right = lambda a, b: jnp.dot(a, b, precision=(highest, lax.Precision.DEFAULT))
    moments = onehot_right(right_side, slot_table.T)
    diag_moments = onehot_right(right_side * self_diag[None, :], slot_table.T)
    own_part = diag_moments + dot(self_trans, moments)
    untranslated = moments
    moments = dot(far_trans, moments)
    g = group_count
    filler = jnp.zeros((g, g), jnp.float32)
    payload = jnp.concatenate(
        [
            jnp.concatenate([moments, own_part, jnp.zeros_like(moments)], axis=1),
            select_mat,
            jnp.concatenate([counts[:, None], jnp.zeros((g, 3 * g - 1), jnp.float32)], axis=1),
        ],
        axis=0,
    )
    rows = moments.shape[0]
    payload, moments = lax.optimization_barrier((payload, moments))
    below = shifted(payload, DEVICES, 1)
    above = shifted(payload, DEVICES, -1)
    two_below = shifted(moments, DEVICES, 2)
    two_above = shifted(moments, DEVICES, -2)
    unpack = lambda block: (
        block[:rows, :g],
        block[:rows, g : 2 * g],
        block[rows : rows + g],
        block[rows + g :, 0],
    )
    moments_below, part_below, select_below, counts_below = unpack(below)
    moments_above, part_above, select_above, counts_above = unpack(above)
    wide = jnp.concatenate([two_below, moments_below, moments, moments_above, two_above], axis=1)
    wide_select = jnp.concatenate(
        [
            jnp.concatenate([select_below, filler, filler], axis=1),
            jnp.concatenate([filler, select_mat, filler], axis=1),
            jnp.concatenate([filler, filler, select_above], axis=1),
        ],
        axis=0,
    )
    local_near = dot(wide, wide_select.T)
    near_counts = jnp.concatenate([counts_below, counts, counts_above])
    near_part = jnp.concatenate([part_below, own_part, part_above], axis=1)
    near_moments = near_part + near_counts[None, :] * local_near
    once = local_part(right_side, self_diag, self_trans)
    twice = local_part(once, self_diag, self_trans)
    column_sums = jnp.stack(
        [
            jnp.sum(a * b, axis=0)
            for a, b in (
                (right_side, right_side),
                (right_side, once),
                (right_side, twice),
                (once, once),
                (once, twice),
                (twice, twice),
            )
        ]
    )
    diag_once = onehot_right(once * self_diag[None, :], slot_table.T)
    twice_sums = onehot_right(twice, slot_table.T)
    diag_twice = onehot_right(twice * self_diag[None, :], slot_table.T)
    diag_sums = onehot_right(self_diag[None, :], slot_table.T)[0]
    diag_squares = onehot_right((self_diag * self_diag)[None, :], slot_table.T)[0]
    first_far = local_near[:, g : 2 * g]
    second_far = dot(far_trans, dot(near_moments, select_mat.T))
    shared = dot(self_trans, first_far) + second_far
    far_sq = first_far * first_far
    far_shared = first_far * shared
    group_terms = jnp.stack(
        [
            jnp.zeros_like(first_far),
            untranslated * first_far,
            diag_moments * first_far + untranslated * shared,
            2.0 * own_part * first_far + counts[None, :] * far_sq,
            (diag_once + twice_sums) * first_far
            + own_part * shared
            + diag_sums[None, :] * far_sq
            + counts[None, :] * far_shared,
            2.0 * diag_twice * first_far
            + 2.0 * twice_sums * shared
            + diag_squares[None, :] * far_sq
            + 2.0 * diag_sums[None, :] * far_shared
            + counts[None, :] * shared * shared,
        ]
    )
    partials = jnp.sum(column_sums, axis=1) + jnp.sum(group_terms, axis=(1, 2))
    first = once + onehot_right(first_far, slot_table)
    totals = all_sum(partials)
    lanes = lax.optimization_barrier(jnp.broadcast_to(totals[:, None], (len(GRAM_PAIRS), 128)))
    g00, g01, g02, g11, g12, g22 = [lanes[k] for k in range(len(GRAM_PAIRS))]
    beta_norm = jnp.sqrt(g00)
    h00 = g01 / g00
    h10 = jnp.sqrt(g11 / g00 - h00 * h00)
    scale = beta_norm * h10
    h01 = (g02 - h00 * g01) / (beta_norm * scale)
    h11 = (g12 - h00 * g11 - h00 * g02 + h00 * h00 * g01) / (scale * scale)
    ww1 = (g22 - 2.0 * h00 * g12 + h00 * h00 * g11) / (scale * scale)
    h21 = jnp.sqrt(ww1 - h01 * h01 - h11 * h11)
    zero = jnp.zeros_like(h00)
    y0, y1 = least_squares(((h00, h01), (h10, h11), (zero, h21)), beta_norm)
    c1 = y1 / scale
    c0 = y0 / beta_norm - c1 * h00
    c0, c1 = lax.optimization_barrier((c0, c1))
    return c0[0] * right_side + c1[0] * first


def solution(mesh):
    placed = (
        P(None, DEVICES),
        P(DEVICES),
        P(DEVICES, None),
        P(DEVICES, None),
        P(DEVICES),
        P(),
        P(),
    )
    return jax.shard_map(
        on_device, mesh=mesh, in_specs=placed, out_specs=P(None, DEVICES), check_vma=False
    )
```

```python
import jax
import jax.numpy as jnp
from jax import lax
from jax.sharding import PartitionSpec as P

ITERS = 2
DEVICES = ("curve", "coef")
GRAM_PAIRS = ((0, 0), (0, 1), (0, 2), (1, 1), (1, 2), (2, 2))


def shifted(array, axis, by):
    peers = lax.axis_size(axis)
    pairs = [(i, i + by) for i in range(peers) if 0 <= i + by < peers]
    return lax.ppermute(array, axis, pairs)


def all_sum(value):
    for axis in ("coef", "curve"):
        peers = lax.axis_size(axis)
        spread = jnp.broadcast_to(value[None, :], (peers,) + value.shape)
        value = jnp.sum(lax.all_to_all(spread, axis, 0, 0, tiled=True), axis=0)
    return value


def local_part(field, self_diag, self_trans):
    highest = lax.Precision.HIGHEST
    return self_diag[None, :] * field + jnp.dot(self_trans, field, precision=highest)


def least_squares(hessen, beta_norm):
    (h00, h01), (h10, h11), (h20, h21) = hessen
    g00 = h00 * h00 + h10 * h10 + h20 * h20
    g01 = h00 * h01 + h10 * h11 + h20 * h21
    g11 = h01 * h01 + h11 * h11 + h21 * h21
    l00 = jnp.sqrt(g00)
    l10 = g01 / l00
    l11 = jnp.sqrt(g11 - l10 * l10)
    f0 = beta_norm * h00 / l00
    f1 = (beta_norm * h01 - l10 * f0) / l11
    y1 = f1 / l11
    y0 = (f0 - l10 * y1) / l00
    return y0, y1


def on_device(right_side, group_ids, pair_sources, pair_weights, self_diag, self_trans, far_trans):
    group_count = pair_sources.shape[0]
    base_group = lax.axis_index(DEVICES) * group_count
    slots = group_ids - base_group
    slot_table = (slots[None, :] == jnp.arange(group_count, dtype=jnp.int32)[:, None]).astype(
        jnp.float32
    )
    columns = base_group - group_count + jnp.arange(3 * group_count, dtype=jnp.int32)
    matches = (pair_sources[:, :, None] == columns[None, None, :]).astype(jnp.float32)
    select_mat = jnp.sum(pair_weights[:, :, None] * matches, axis=1)
    counts = jnp.sum(slot_table, axis=1)
    select_mat, counts, right_side = lax.optimization_barrier((select_mat, counts, right_side))
    highest = lax.Precision.HIGHEST
    dot = lambda a, b: jnp.dot(a, b, precision=highest)
    moments = dot(right_side, slot_table.T)
    own_part = dot(right_side * self_diag[None, :], slot_table.T) + dot(self_trans, moments)
    moments = dot(far_trans, moments)
    g = group_count
    filler = jnp.zeros((g, g), jnp.float32)
    payload = jnp.concatenate(
        [
            jnp.concatenate([moments, own_part, jnp.zeros_like(moments)], axis=1),
            select_mat,
            jnp.concatenate([counts[:, None], jnp.zeros((g, 3 * g - 1), jnp.float32)], axis=1),
        ],
        axis=0,
    )
    rows = moments.shape[0]
    payload, moments = lax.optimization_barrier((payload, moments))
    below = shifted(payload, DEVICES, 1)
    above = shifted(payload, DEVICES, -1)
    two_below = shifted(moments, DEVICES, 2)
    two_above = shifted(moments, DEVICES, -2)
    unpack = lambda block: (
        block[:rows, :g],
        block[:rows, g : 2 * g],
        block[rows : rows + g],
        block[rows + g :, 0],
    )
    moments_below, part_below, select_below, counts_below = unpack(below)
    moments_above, part_above, select_above, counts_above = unpack(above)
    wide = jnp.concatenate([two_below, moments_below, moments, moments_above, two_above], axis=1)
    wide_select = jnp.concatenate(
        [
            jnp.concatenate([select_below, filler, filler], axis=1),
            jnp.concatenate([filler, select_mat, filler], axis=1),
            jnp.concatenate([filler, filler, select_above], axis=1),
        ],
        axis=0,
    )
    local_near = dot(wide, wide_select.T)
    near_counts = jnp.concatenate([counts_below, counts, counts_above])
    near_part = jnp.concatenate([part_below, own_part, part_above], axis=1)
    near_moments = near_part + near_counts[None, :] * local_near
    first = local_part(right_side, self_diag, self_trans) + dot(local_near[:, g : 2 * g], slot_table)
    local_next = dot(far_trans, dot(near_moments, select_mat.T))
    second = local_part(first, self_diag, self_trans) + dot(local_next, slot_table)
    krylov = (right_side, first, second)
    columns_sums = jnp.stack([jnp.sum(krylov[i] * krylov[j], axis=0) for i, j in GRAM_PAIRS])
    partials = jnp.sum(columns_sums, axis=1)
    totals = all_sum(partials)
    lanes = lax.optimization_barrier(jnp.broadcast_to(totals[:, None], (len(GRAM_PAIRS), 128)))
    g00, g01, g02, g11, g12, g22 = [lanes[k] for k in range(len(GRAM_PAIRS))]
    beta_norm = jnp.sqrt(g00)
    h00 = g01 / g00
    h10 = jnp.sqrt(g11 / g00 - h00 * h00)
    scale = beta_norm * h10
    h01 = (g02 - h00 * g01) / (beta_norm * scale)
    h11 = (g12 - h00 * g11 - h00 * g02 + h00 * h00 * g01) / (scale * scale)
    ww1 = (g22 - 2.0 * h00 * g12 + h00 * h00 * g11) / (scale * scale)
    h21 = jnp.sqrt(ww1 - h01 * h01 - h11 * h11)
    zero = jnp.zeros_like(h00)
    y0, y1 = least_squares(((h00, h01), (h10, h11), (zero, h21)), beta_norm)
    c1 = y1 / scale
    c0 = y0 / beta_norm - c1 * h00
    c0, c1 = lax.optimization_barrier((c0, c1))
    return c0[0] * right_side + c1[0] * first


def solution(mesh):
    placed = (
        P(None, DEVICES),
        P(DEVICES),
        P(DEVICES, None),
        P(DEVICES, None),
        P(DEVICES),
        P(),
        P(),
    )
    return jax.shard_map(
        on_device, mesh=mesh, in_specs=placed, out_specs=P(None, DEVICES), check_vma=False
    )
```

```python
import jax
import jax.numpy as jnp
from jax import lax
from jax.sharding import PartitionSpec as P

ITERS = 2
DEVICES = ("curve", "coef")
GRAM_PAIRS = ((0, 0), (0, 1), (0, 2), (1, 1), (1, 2), (2, 2))


def shifted(array, axis, by):
    peers = lax.axis_size(axis)
    pairs = [(i, i + by) for i in range(peers) if 0 <= i + by < peers]
    return lax.ppermute(array, axis, pairs)


def all_sum(value):
    for axis in ("curve", "coef"):
        peers = lax.axis_size(axis)
        spread = jnp.broadcast_to(value[None, :], (peers,) + value.shape)
        value = jnp.sum(lax.all_to_all(spread, axis, 0, 0, tiled=True), axis=0)
    return value


def local_part(field, self_diag, self_trans):
    highest = lax.Precision.HIGHEST
    return self_diag[None, :] * field + jnp.dot(self_trans, field, precision=highest)


def least_squares(hessen, beta_norm):
    (h00, h01), (h10, h11), (h20, h21) = hessen
    g00 = h00 * h00 + h10 * h10 + h20 * h20
    g01 = h00 * h01 + h10 * h11 + h20 * h21
    g11 = h01 * h01 + h11 * h11 + h21 * h21
    l00 = jnp.sqrt(g00)
    l10 = g01 / l00
    l11 = jnp.sqrt(g11 - l10 * l10)
    f0 = beta_norm * h00 / l00
    f1 = (beta_norm * h01 - l10 * f0) / l11
    y1 = f1 / l11
    y0 = (f0 - l10 * y1) / l00
    return y0, y1


def on_device(right_side, group_ids, pair_sources, pair_weights, self_diag, self_trans, far_trans):
    group_count = pair_sources.shape[0]
    base_group = lax.axis_index(DEVICES) * group_count
    slots = group_ids - base_group
    slot_table = (slots[None, :] == jnp.arange(group_count, dtype=jnp.int32)[:, None]).astype(
        jnp.float32
    )
    columns = base_group - group_count + jnp.arange(3 * group_count, dtype=jnp.int32)
    matches = (pair_sources[:, :, None] == columns[None, None, :]).astype(jnp.float32)
    select_mat = jnp.sum(pair_weights[:, :, None] * matches, axis=1)
    counts = jnp.sum(slot_table, axis=1)
    highest = lax.Precision.HIGHEST
    dot = lambda a, b: jnp.dot(a, b, precision=highest)
    moments = dot(right_side, slot_table.T)
    own_part = dot(right_side * self_diag[None, :], slot_table.T) + dot(self_trans, moments)
    moments = dot(far_trans, moments)
    g = group_count
    filler = jnp.zeros((g, g), jnp.float32)
    payload = jnp.concatenate(
        [
            jnp.concatenate([moments, own_part, jnp.zeros_like(moments)], axis=1),
            select_mat,
            jnp.concatenate([counts[:, None], jnp.zeros((g, 3 * g - 1), jnp.float32)], axis=1),
        ],
        axis=0,
    )
    rows = moments.shape[0]
    payload, moments = lax.optimization_barrier((payload, moments))
    below = shifted(payload, DEVICES, 1)
    above = shifted(payload, DEVICES, -1)
    two_below = shifted(moments, DEVICES, 2)
    two_above = shifted(moments, DEVICES, -2)
    unpack = lambda block: (
        block[:rows, :g],
        block[:rows, g : 2 * g],
        block[rows : rows + g],
        block[rows + g :, 0],
    )
    moments_below, part_below, select_below, counts_below = unpack(below)
    moments_above, part_above, select_above, counts_above = unpack(above)
    wide = jnp.concatenate([two_below, moments_below, moments, moments_above, two_above], axis=1)
    wide_select = jnp.concatenate(
        [
            jnp.concatenate([select_below, filler, filler], axis=1),
            jnp.concatenate([filler, select_mat, filler], axis=1),
            jnp.concatenate([filler, filler, select_above], axis=1),
        ],
        axis=0,
    )
    local_near = dot(wide, wide_select.T)
    near_counts = jnp.concatenate([counts_below, counts, counts_above])
    near_part = jnp.concatenate([part_below, own_part, part_above], axis=1)
    near_moments = near_part + near_counts[None, :] * local_near
    first = local_part(right_side, self_diag, self_trans) + dot(local_near[:, g : 2 * g], slot_table)
    local_next = dot(far_trans, dot(near_moments, select_mat.T))
    second = local_part(first, self_diag, self_trans) + dot(local_next, slot_table)
    krylov = (right_side, first, second)
    columns_sums = jnp.stack([jnp.sum(krylov[i] * krylov[j], axis=0) for i, j in GRAM_PAIRS])
    partials = jnp.sum(columns_sums, axis=1)
    totals = all_sum(partials)
    lanes = lax.optimization_barrier(jnp.broadcast_to(totals[:, None], (len(GRAM_PAIRS), 128)))
    g00, g01, g02, g11, g12, g22 = [lanes[k] for k in range(len(GRAM_PAIRS))]
    beta_norm = jnp.sqrt(g00)
    h00 = g01 / g00
    h10 = jnp.sqrt(g11 / g00 - h00 * h00)
    scale = beta_norm * h10
    h01 = (g02 - h00 * g01) / (beta_norm * scale)
    h11 = (g12 - h00 * g11 - h00 * g02 + h00 * h00 * g01) / (scale * scale)
    ww1 = (g22 - 2.0 * h00 * g12 + h00 * h00 * g11) / (scale * scale)
    h21 = jnp.sqrt(ww1 - h01 * h01 - h11 * h11)
    zero = jnp.zeros_like(h00)
    y0, y1 = least_squares(((h00, h01), (h10, h11), (zero, h21)), beta_norm)
    c1 = y1 / scale
    c0 = y0 / beta_norm - c1 * h00
    c0, c1 = lax.optimization_barrier((c0, c1))
    return c0[0] * right_side + c1[0] * first


def solution(mesh):
    placed = (
        P(None, DEVICES),
        P(DEVICES),
        P(DEVICES, None),
        P(DEVICES, None),
        P(DEVICES),
        P(),
        P(),
    )
    return jax.shard_map(
        on_device, mesh=mesh, in_specs=placed, out_specs=P(None, DEVICES), check_vma=False
    )
```

```python
import jax
import jax.numpy as jnp
from jax import lax
from jax.sharding import PartitionSpec as P

ITERS = 2
DEVICES = ("curve", "coef")
GRAM_PAIRS = ((0, 0), (0, 1), (0, 2), (1, 1), (1, 2), (2, 2))


def shifted(array, axis, by):
    peers = lax.axis_size(axis)
    pairs = [(i, i + by) for i in range(peers) if 0 <= i + by < peers]
    return lax.ppermute(array, axis, pairs)


def all_sum(value):
    for axis in ("coef", "curve"):
        peers = lax.axis_size(axis)
        spread = jnp.broadcast_to(value[None, :], (peers,) + value.shape)
        value = jnp.sum(lax.all_to_all(spread, axis, 0, 0, tiled=True), axis=0)
    return value


def local_part(field, self_diag, self_trans):
    highest = lax.Precision.HIGHEST
    return self_diag[None, :] * field + jnp.dot(self_trans, field, precision=highest)


def least_squares(hessen, beta_norm):
    (h00, h01), (h10, h11), (h20, h21) = hessen
    g00 = h00 * h00 + h10 * h10 + h20 * h20
    g01 = h00 * h01 + h10 * h11 + h20 * h21
    g11 = h01 * h01 + h11 * h11 + h21 * h21
    l00 = jnp.sqrt(g00)
    l10 = g01 / l00
    l11 = jnp.sqrt(g11 - l10 * l10)
    f0 = beta_norm * h00 / l00
    f1 = (beta_norm * h01 - l10 * f0) / l11
    y1 = f1 / l11
    y0 = (f0 - l10 * y1) / l00
    return y0, y1


def on_device(right_side, group_ids, pair_sources, pair_weights, self_diag, self_trans, far_trans):
    group_count = pair_sources.shape[0]
    base_group = lax.axis_index(DEVICES) * group_count
    slots = group_ids - base_group
    slot_table = (slots[None, :] == jnp.arange(group_count, dtype=jnp.int32)[:, None]).astype(
        jnp.float32
    )
    columns = base_group - group_count + jnp.arange(3 * group_count, dtype=jnp.int32)
    matches = (pair_sources[:, :, None] == columns[None, None, :]).astype(jnp.float32)
    select_mat = jnp.sum(pair_weights[:, :, None] * matches, axis=1)
    counts = jnp.sum(slot_table, axis=1)
    highest = lax.Precision.HIGHEST
    dot = lambda a, b: jnp.dot(a, b, precision=highest)
    fields = jnp.concatenate([right_side, right_side * self_diag[None, :]], axis=0)
    high = fields.astype(jnp.bfloat16)
    rest = fields - high.astype(jnp.float32)
    middle = rest.astype(jnp.bfloat16)
    low = (rest - middle.astype(jnp.float32)).astype(jnp.bfloat16)
    parts = jnp.concatenate([high, middle, low], axis=0)
    sums = jnp.dot(parts, slot_table.T.astype(jnp.bfloat16), preferred_element_type=jnp.float32)
    sums = sums.reshape((3,) + fields.shape[:1] + sums.shape[1:]).sum(axis=0)
    rows = right_side.shape[0]
    moments = sums[:rows]
    own_part = sums[rows:] + dot(self_trans, moments)
    moments = dot(far_trans, moments)
    g = group_count
    filler = jnp.zeros((g, g), jnp.float32)
    payload = jnp.concatenate(
        [
            jnp.concatenate([moments, own_part, jnp.zeros_like(moments)], axis=1),
            select_mat,
            jnp.concatenate([counts[:, None], jnp.zeros((g, 3 * g - 1), jnp.float32)], axis=1),
        ],
        axis=0,
    )
    payload, moments = lax.optimization_barrier((payload, moments))
    below = shifted(payload, DEVICES, 1)
    above = shifted(payload, DEVICES, -1)
    two_below = shifted(moments, DEVICES, 2)
    two_above = shifted(moments, DEVICES, -2)
    unpack = lambda block: (
        block[:rows, :g],
        block[:rows, g : 2 * g],
        block[rows : rows + g],
        block[rows + g :, 0],
    )
    moments_below, part_below, select_below, counts_below = unpack(below)
    moments_above, part_above, select_above, counts_above = unpack(above)
    wide = jnp.concatenate([two_below, moments_below, moments, moments_above, two_above], axis=1)
    wide_select = jnp.concatenate(
        [
            jnp.concatenate([select_below, filler, filler], axis=1),
            jnp.concatenate([filler, select_mat, filler], axis=1),
            jnp.concatenate([filler, filler, select_above], axis=1),
        ],
        axis=0,
    )
    local_near = dot(wide, wide_select.T)
    near_counts = jnp.concatenate([counts_below, counts, counts_above])
    near_part = jnp.concatenate([part_below, own_part, part_above], axis=1)
    near_moments = near_part + near_counts[None, :] * local_near
    first = local_part(right_side, self_diag, self_trans) + dot(local_near[:, g : 2 * g], slot_table)
    local_next = dot(far_trans, dot(near_moments, select_mat.T))
    second = local_part(first, self_diag, self_trans) + dot(local_next, slot_table)
    krylov = (right_side, first, second)
    columns_sums = jnp.stack([jnp.sum(krylov[i] * krylov[j], axis=0) for i, j in GRAM_PAIRS])
    partials = jnp.sum(columns_sums, axis=1)
    totals = all_sum(partials)
    lanes = lax.optimization_barrier(jnp.broadcast_to(totals[:, None], (len(GRAM_PAIRS), 128)))
    g00, g01, g02, g11, g12, g22 = [lanes[k] for k in range(len(GRAM_PAIRS))]
    beta_norm = jnp.sqrt(g00)
    h00 = g01 / g00
    h10 = jnp.sqrt(g11 / g00 - h00 * h00)
    scale = beta_norm * h10
    h01 = (g02 - h00 * g01) / (beta_norm * scale)
    h11 = (g12 - h00 * g11 - h00 * g02 + h00 * h00 * g01) / (scale * scale)
    ww1 = (g22 - 2.0 * h00 * g12 + h00 * h00 * g11) / (scale * scale)
    h21 = jnp.sqrt(ww1 - h01 * h01 - h11 * h11)
    zero = jnp.zeros_like(h00)
    y0, y1 = least_squares(((h00, h01), (h10, h11), (zero, h21)), beta_norm)
    c1 = y1 / scale
    c0 = y0 / beta_norm - c1 * h00
    c0, c1 = lax.optimization_barrier((c0, c1))
    return c0[0] * right_side + c1[0] * first


def solution(mesh):
    placed = (
        P(None, DEVICES),
        P(DEVICES),
        P(DEVICES, None),
        P(DEVICES, None),
        P(DEVICES),
        P(),
        P(),
    )
    return jax.shard_map(
        on_device, mesh=mesh, in_specs=placed, out_specs=P(None, DEVICES), check_vma=False
    )
```

```python
import jax
import jax.numpy as jnp
from jax import lax
from jax.sharding import PartitionSpec as P

ITERS = 2
DEVICES = ("curve", "coef")
GRAM_PAIRS = ((0, 0), (0, 1), (0, 2), (1, 1), (1, 2), (2, 2))


def shifted(array, axis, by):
    peers = lax.axis_size(axis)
    pairs = [(i, i + by) for i in range(peers) if 0 <= i + by < peers]
    return lax.ppermute(array, axis, pairs)


def all_sum(value):
    for axis in ("coef", "curve"):
        peers = lax.axis_size(axis)
        spread = jnp.broadcast_to(value[None, :], (peers,) + value.shape)
        value = jnp.sum(lax.all_to_all(spread, axis, 0, 0, tiled=True), axis=0)
    return value


def local_part(field, self_diag, self_trans):
    highest = lax.Precision.HIGHEST
    return self_diag[None, :] * field + jnp.dot(self_trans, field, precision=highest)


def least_squares(hessen, beta_norm):
    (h00, h01), (h10, h11), (h20, h21) = hessen
    g00 = h00 * h00 + h10 * h10 + h20 * h20
    g01 = h00 * h01 + h10 * h11 + h20 * h21
    g11 = h01 * h01 + h11 * h11 + h21 * h21
    l00 = jnp.sqrt(g00)
    l10 = g01 / l00
    l11 = jnp.sqrt(g11 - l10 * l10)
    f0 = beta_norm * h00 / l00
    f1 = (beta_norm * h01 - l10 * f0) / l11
    y1 = f1 / l11
    y0 = (f0 - l10 * y1) / l00
    return y0, y1


def on_device(right_side, group_ids, pair_sources, pair_weights, self_diag, self_trans, far_trans):
    group_count = pair_sources.shape[0]
    base_group = lax.axis_index(DEVICES) * group_count
    slots = group_ids - base_group
    slot_table = (slots[None, :] == jnp.arange(group_count, dtype=jnp.int32)[:, None]).astype(
        jnp.float32
    )
    columns = base_group - group_count + jnp.arange(3 * group_count, dtype=jnp.int32)
    matches = (pair_sources[:, :, None] == columns[None, None, :]).astype(jnp.float32)
    select_mat = jnp.sum(pair_weights[:, :, None] * matches, axis=1)
    counts = jnp.sum(slot_table, axis=1)
    highest = lax.Precision.HIGHEST
    dot = lambda a, b: jnp.dot(a, b, precision=highest)
    fields = jnp.concatenate([right_side, right_side * self_diag[None, :]], axis=0)
    to_bf16 = lambda x: lax.reduce_precision(x, exponent_bits=8, mantissa_bits=7)
    high = to_bf16(fields)
    rest = fields - high
    middle = to_bf16(rest)
    low = rest - middle
    parts = jnp.concatenate([high, middle, low], axis=0).astype(jnp.bfloat16)
    sums = jnp.dot(parts, slot_table.T.astype(jnp.bfloat16), preferred_element_type=jnp.float32)
    sums = sums.reshape((3,) + fields.shape[:1] + sums.shape[1:]).sum(axis=0)
    rows = right_side.shape[0]
    moments = sums[:rows]
    own_part = sums[rows:] + dot(self_trans, moments)
    moments = dot(far_trans, moments)
    g = group_count
    filler = jnp.zeros((g, g), jnp.float32)
    payload = jnp.concatenate(
        [
            jnp.concatenate([moments, own_part, jnp.zeros_like(moments)], axis=1),
            select_mat,
            jnp.concatenate([counts[:, None], jnp.zeros((g, 3 * g - 1), jnp.float32)], axis=1),
        ],
        axis=0,
    )
    payload, moments = lax.optimization_barrier((payload, moments))
    below = shifted(payload, DEVICES, 1)
    above = shifted(payload, DEVICES, -1)
    two_below = shifted(moments, DEVICES, 2)
    two_above = shifted(moments, DEVICES, -2)
    unpack = lambda block: (
        block[:rows, :g],
        block[:rows, g : 2 * g],
        block[rows : rows + g],
        block[rows + g :, 0],
    )
    moments_below, part_below, select_below, counts_below = unpack(below)
    moments_above, part_above, select_above, counts_above = unpack(above)
    wide = jnp.concatenate([two_below, moments_below, moments, moments_above, two_above], axis=1)
    wide_select = jnp.concatenate(
        [
            jnp.concatenate([select_below, filler, filler], axis=1),
            jnp.concatenate([filler, select_mat, filler], axis=1),
            jnp.concatenate([filler, filler, select_above], axis=1),
        ],
        axis=0,
    )
    local_near = dot(wide, wide_select.T)
    near_counts = jnp.concatenate([counts_below, counts, counts_above])
    near_part = jnp.concatenate([part_below, own_part, part_above], axis=1)
    near_moments = near_part + near_counts[None, :] * local_near
    first = local_part(right_side, self_diag, self_trans) + dot(local_near[:, g : 2 * g], slot_table)
    local_next = dot(far_trans, dot(near_moments, select_mat.T))
    second = local_part(first, self_diag, self_trans) + dot(local_next, slot_table)
    krylov = (right_side, first, second)
    columns_sums = jnp.stack([jnp.sum(krylov[i] * krylov[j], axis=0) for i, j in GRAM_PAIRS])
    partials = jnp.sum(columns_sums, axis=1)
    totals = all_sum(partials)
    lanes = lax.optimization_barrier(jnp.broadcast_to(totals[:, None], (len(GRAM_PAIRS), 128)))
    g00, g01, g02, g11, g12, g22 = [lanes[k] for k in range(len(GRAM_PAIRS))]
    beta_norm = jnp.sqrt(g00)
    h00 = g01 / g00
    h10 = jnp.sqrt(g11 / g00 - h00 * h00)
    scale = beta_norm * h10
    h01 = (g02 - h00 * g01) / (beta_norm * scale)
    h11 = (g12 - h00 * g11 - h00 * g02 + h00 * h00 * g01) / (scale * scale)
    ww1 = (g22 - 2.0 * h00 * g12 + h00 * h00 * g11) / (scale * scale)
    h21 = jnp.sqrt(ww1 - h01 * h01 - h11 * h11)
    zero = jnp.zeros_like(h00)
    y0, y1 = least_squares(((h00, h01), (h10, h11), (zero, h21)), beta_norm)
    c1 = y1 / scale
    c0 = y0 / beta_norm - c1 * h00
    c0, c1 = lax.optimization_barrier((c0, c1))
    return c0[0] * right_side + c1[0] * first


def solution(mesh):
    placed = (
        P(None, DEVICES),
        P(DEVICES),
        P(DEVICES, None),
        P(DEVICES, None),
        P(DEVICES),
        P(),
        P(),
    )
    return jax.shard_map(
        on_device, mesh=mesh, in_specs=placed, out_specs=P(None, DEVICES), check_vma=False
    )
```

```python
import jax
import jax.numpy as jnp
from jax import lax
from jax.sharding import PartitionSpec as P

ITERS = 2
DEVICES = ("curve", "coef")
GRAM_PAIRS = ((0, 0), (0, 1), (0, 2), (1, 1), (1, 2), (2, 2))


def shifted(array, axis, by):
    peers = lax.axis_size(axis)
    pairs = [(i, i + by) for i in range(peers) if 0 <= i + by < peers]
    return lax.ppermute(array, axis, pairs)


def all_sum(value):
    for axis in ("coef", "curve"):
        peers = lax.axis_size(axis)
        spread = jnp.broadcast_to(value[None, :], (peers,) + value.shape)
        value = jnp.sum(lax.all_to_all(spread, axis, 0, 0, tiled=True), axis=0)
    return value


def local_part(field, self_diag, self_trans):
    highest = lax.Precision.HIGHEST
    return self_diag[None, :] * field + jnp.dot(self_trans, field, precision=highest)


def least_squares(hessen, beta_norm):
    (h00, h01), (h10, h11), (h20, h21) = hessen
    g00 = h00 * h00 + h10 * h10 + h20 * h20
    g01 = h00 * h01 + h10 * h11 + h20 * h21
    g11 = h01 * h01 + h11 * h11 + h21 * h21
    l00 = jnp.sqrt(g00)
    l10 = g01 / l00
    l11 = jnp.sqrt(g11 - l10 * l10)
    f0 = beta_norm * h00 / l00
    f1 = (beta_norm * h01 - l10 * f0) / l11
    y1 = f1 / l11
    y0 = (f0 - l10 * y1) / l00
    return y0, y1


def on_device(right_side, group_ids, pair_sources, pair_weights, self_diag, self_trans, far_trans):
    group_count = pair_sources.shape[0]
    base_group = lax.axis_index(DEVICES) * group_count
    slots = group_ids - base_group
    slot_table = (slots[None, :] == jnp.arange(group_count, dtype=jnp.int32)[:, None]).astype(
        jnp.float32
    )
    columns = base_group - group_count + jnp.arange(3 * group_count, dtype=jnp.int32)
    matches = (pair_sources[:, :, None] == columns[None, None, :]).astype(jnp.float32)
    select_mat = jnp.sum(pair_weights[:, :, None] * matches, axis=1)
    counts = jnp.sum(slot_table, axis=1)
    highest = lax.Precision.HIGHEST
    dot = lambda a, b: jnp.dot(a, b, precision=highest)
    onehot = lambda a, b: jnp.dot(a, b, precision=lax.Precision.HIGH)
    moments = onehot(right_side, slot_table.T)
    own_part = onehot(right_side * self_diag[None, :], slot_table.T) + dot(self_trans, moments)
    moments = dot(far_trans, moments)
    g = group_count
    filler = jnp.zeros((g, g), jnp.float32)
    payload = jnp.concatenate(
        [
            jnp.concatenate([moments, own_part, jnp.zeros_like(moments)], axis=1),
            select_mat,
            jnp.concatenate([counts[:, None], jnp.zeros((g, 3 * g - 1), jnp.float32)], axis=1),
        ],
        axis=0,
    )
    rows = moments.shape[0]
    payload, moments = lax.optimization_barrier((payload, moments))
    below = shifted(payload, DEVICES, 1)
    above = shifted(payload, DEVICES, -1)
    two_below = shifted(moments, DEVICES, 2)
    two_above = shifted(moments, DEVICES, -2)
    unpack = lambda block: (
        block[:rows, :g],
        block[:rows, g : 2 * g],
        block[rows : rows + g],
        block[rows + g :, 0],
    )
    moments_below, part_below, select_below, counts_below = unpack(below)
    moments_above, part_above, select_above, counts_above = unpack(above)
    wide = jnp.concatenate([two_below, moments_below, moments, moments_above, two_above], axis=1)
    wide_select = jnp.concatenate(
        [
            jnp.concatenate([select_below, filler, filler], axis=1),
            jnp.concatenate([filler, select_mat, filler], axis=1),
            jnp.concatenate([filler, filler, select_above], axis=1),
        ],
        axis=0,
    )
    local_near = dot(wide, wide_select.T)
    near_counts = jnp.concatenate([counts_below, counts, counts_above])
    near_part = jnp.concatenate([part_below, own_part, part_above], axis=1)
    near_moments = near_part + near_counts[None, :] * local_near
    first = local_part(right_side, self_diag, self_trans) + onehot(local_near[:, g : 2 * g], slot_table)
    local_next = dot(far_trans, dot(near_moments, select_mat.T))
    second = local_part(first, self_diag, self_trans) + onehot(local_next, slot_table)
    krylov = (right_side, first, second)
    columns_sums = jnp.stack([jnp.sum(krylov[i] * krylov[j], axis=0) for i, j in GRAM_PAIRS])
    partials = jnp.sum(columns_sums, axis=1)
    totals = all_sum(partials)
    lanes = lax.optimization_barrier(jnp.broadcast_to(totals[:, None], (len(GRAM_PAIRS), 128)))
    g00, g01, g02, g11, g12, g22 = [lanes[k] for k in range(len(GRAM_PAIRS))]
    beta_norm = jnp.sqrt(g00)
    h00 = g01 / g00
    h10 = jnp.sqrt(g11 / g00 - h00 * h00)
    scale = beta_norm * h10
    h01 = (g02 - h00 * g01) / (beta_norm * scale)
    h11 = (g12 - h00 * g11 - h00 * g02 + h00 * h00 * g01) / (scale * scale)
    ww1 = (g22 - 2.0 * h00 * g12 + h00 * h00 * g11) / (scale * scale)
    h21 = jnp.sqrt(ww1 - h01 * h01 - h11 * h11)
    zero = jnp.zeros_like(h00)
    y0, y1 = least_squares(((h00, h01), (h10, h11), (zero, h21)), beta_norm)
    c1 = y1 / scale
    c0 = y0 / beta_norm - c1 * h00
    c0, c1 = lax.optimization_barrier((c0, c1))
    return c0[0] * right_side + c1[0] * first


def solution(mesh):
    placed = (
        P(None, DEVICES),
        P(DEVICES),
        P(DEVICES, None),
        P(DEVICES, None),
        P(DEVICES),
        P(),
        P(),
    )
    return jax.shard_map(
        on_device, mesh=mesh, in_specs=placed, out_specs=P(None, DEVICES), check_vma=False
    )
```

```python
import jax
import jax.numpy as jnp
from jax import lax
from jax.sharding import PartitionSpec as P

ITERS = 2
DEVICES = ("curve", "coef")
GRAM_PAIRS = ((0, 0), (0, 1), (0, 2), (1, 1), (1, 2), (2, 2))


def shifted(array, axis, by):
    peers = lax.axis_size(axis)
    pairs = [(i, i + by) for i in range(peers) if 0 <= i + by < peers]
    return lax.ppermute(array, axis, pairs)


def all_sum(value):
    for axis in ("coef", "curve"):
        peers = lax.axis_size(axis)
        spread = jnp.broadcast_to(value[None, :], (peers,) + value.shape)
        value = jnp.sum(lax.all_to_all(spread, axis, 0, 0, tiled=True), axis=0)
    return value


def local_part(field, self_diag, self_trans):
    highest = lax.Precision.HIGHEST
    return self_diag[None, :] * field + jnp.dot(self_trans, field, precision=highest)


def least_squares(hessen, beta_norm):
    (h00, h01), (h10, h11), (h20, h21) = hessen
    g00 = h00 * h00 + h10 * h10 + h20 * h20
    g01 = h00 * h01 + h10 * h11 + h20 * h21
    g11 = h01 * h01 + h11 * h11 + h21 * h21
    l00 = jnp.sqrt(g00)
    l10 = g01 / l00
    l11 = jnp.sqrt(g11 - l10 * l10)
    f0 = beta_norm * h00 / l00
    f1 = (beta_norm * h01 - l10 * f0) / l11
    y1 = f1 / l11
    y0 = (f0 - l10 * y1) / l00
    return y0, y1


def on_device(right_side, group_ids, pair_sources, pair_weights, self_diag, self_trans, far_trans):
    group_count = pair_sources.shape[0]
    base_group = lax.axis_index(DEVICES) * group_count
    own_groups = base_group + jnp.arange(group_count, dtype=jnp.int32)
    slot_table = (group_ids[None, :] == own_groups[:, None]).astype(jnp.float32)
    columns = base_group - group_count + jnp.arange(3 * group_count, dtype=jnp.int32)
    matches = (pair_sources[:, :, None] == columns[None, None, :]).astype(jnp.float32)
    select_mat = jnp.sum(pair_weights[:, :, None] * matches, axis=1)
    counts = jnp.sum(slot_table, axis=1)
    highest = lax.Precision.HIGHEST
    dot = lambda a, b: jnp.dot(a, b, precision=highest)
    moments = dot(right_side, slot_table.T)
    own_part = dot(right_side * self_diag[None, :], slot_table.T) + dot(self_trans, moments)
    moments = dot(far_trans, moments)
    g = group_count
    filler = jnp.zeros((g, g), jnp.float32)
    payload = jnp.concatenate(
        [
            jnp.concatenate([moments, own_part, jnp.zeros_like(moments)], axis=1),
            select_mat,
            jnp.concatenate([counts[:, None], jnp.zeros((g, 3 * g - 1), jnp.float32)], axis=1),
        ],
        axis=0,
    )
    rows = moments.shape[0]
    payload, moments = lax.optimization_barrier((payload, moments))
    below = shifted(payload, DEVICES, 1)
    above = shifted(payload, DEVICES, -1)
    two_below = shifted(moments, DEVICES, 2)
    two_above = shifted(moments, DEVICES, -2)
    unpack = lambda block: (
        block[:rows, :g],
        block[:rows, g : 2 * g],
        block[rows : rows + g],
        block[rows + g :, 0],
    )
    moments_below, part_below, select_below, counts_below = unpack(below)
    moments_above, part_above, select_above, counts_above = unpack(above)
    wide = jnp.concatenate([two_below, moments_below, moments, moments_above, two_above], axis=1)
    wide_select = jnp.concatenate(
        [
            jnp.concatenate([select_below, filler, filler], axis=1),
            jnp.concatenate([filler, select_mat, filler], axis=1),
            jnp.concatenate([filler, filler, select_above], axis=1),
        ],
        axis=0,
    )
    local_near = dot(wide, wide_select.T)
    near_counts = jnp.concatenate([counts_below, counts, counts_above])
    near_part = jnp.concatenate([part_below, own_part, part_above], axis=1)
    near_moments = near_part + near_counts[None, :] * local_near
    first = local_part(right_side, self_diag, self_trans) + dot(local_near[:, g : 2 * g], slot_table)
    local_next = dot(far_trans, dot(near_moments, select_mat.T))
    second = local_part(first, self_diag, self_trans) + dot(local_next, slot_table)
    krylov = (right_side, first, second)
    columns_sums = jnp.stack([jnp.sum(krylov[i] * krylov[j], axis=0) for i, j in GRAM_PAIRS])
    partials = jnp.sum(columns_sums, axis=1)
    totals = all_sum(partials)
    lanes = lax.optimization_barrier(jnp.broadcast_to(totals[:, None], (len(GRAM_PAIRS), 128)))
    g00, g01, g02, g11, g12, g22 = [lanes[k] for k in range(len(GRAM_PAIRS))]
    beta_norm = jnp.sqrt(g00)
    h00 = g01 / g00
    h10 = jnp.sqrt(g11 / g00 - h00 * h00)
    scale = beta_norm * h10
    h01 = (g02 - h00 * g01) / (beta_norm * scale)
    h11 = (g12 - h00 * g11 - h00 * g02 + h00 * h00 * g01) / (scale * scale)
    ww1 = (g22 - 2.0 * h00 * g12 + h00 * h00 * g11) / (scale * scale)
    h21 = jnp.sqrt(ww1 - h01 * h01 - h11 * h11)
    zero = jnp.zeros_like(h00)
    y0, y1 = least_squares(((h00, h01), (h10, h11), (zero, h21)), beta_norm)
    c1 = y1 / scale
    c0 = y0 / beta_norm - c1 * h00
    c0, c1 = lax.optimization_barrier((c0, c1))
    return c0[0] * right_side + c1[0] * first


def solution(mesh):
    placed = (
        P(None, DEVICES),
        P(DEVICES),
        P(DEVICES, None),
        P(DEVICES, None),
        P(DEVICES),
        P(),
        P(),
    )
    return jax.shard_map(
        on_device, mesh=mesh, in_specs=placed, out_specs=P(None, DEVICES), check_vma=False
    )
```

```python
import jax
import jax.numpy as jnp
from jax import lax
from jax.sharding import PartitionSpec as P

ITERS = 2
DEVICES = ("curve", "coef")
GRAM_PAIRS = ((0, 0), (0, 1), (0, 2), (1, 1), (1, 2), (2, 2))


def shifted(array, axis, by):
    peers = lax.axis_size(axis)
    pairs = [(i, i + by) for i in range(peers) if 0 <= i + by < peers]
    return lax.ppermute(array, axis, pairs)


def all_sum(value):
    for axis in ("coef", "curve"):
        peers = lax.axis_size(axis)
        spread = jnp.broadcast_to(value[None, :], (peers,) + value.shape)
        value = jnp.sum(lax.all_to_all(spread, axis, 0, 0, tiled=True), axis=0)
    return value


def local_part(field, self_diag, self_trans):
    highest = lax.Precision.HIGHEST
    return self_diag[None, :] * field + jnp.dot(self_trans, field, precision=highest)


def least_squares(hessen, beta_norm):
    (h00, h01), (h10, h11), (h20, h21) = hessen
    g00 = h00 * h00 + h10 * h10 + h20 * h20
    g01 = h00 * h01 + h10 * h11 + h20 * h21
    g11 = h01 * h01 + h11 * h11 + h21 * h21
    l00 = jnp.sqrt(g00)
    l10 = g01 / l00
    l11 = jnp.sqrt(g11 - l10 * l10)
    f0 = beta_norm * h00 / l00
    f1 = (beta_norm * h01 - l10 * f0) / l11
    y1 = f1 / l11
    y0 = (f0 - l10 * y1) / l00
    return y0, y1


def on_device(right_side, group_ids, pair_sources, pair_weights, self_diag, self_trans, far_trans):
    group_count = pair_sources.shape[0]
    base_group = lax.axis_index(DEVICES) * group_count
    slots = group_ids - base_group
    slot_table = (slots[None, :] == jnp.arange(group_count, dtype=jnp.int32)[:, None]).astype(
        jnp.float32
    )
    columns = base_group - group_count + jnp.arange(3 * group_count, dtype=jnp.int32)
    matches = (pair_sources[:, :, None] == columns[None, None, :]).astype(jnp.float32)
    select_mat = jnp.sum(pair_weights[:, :, None] * matches, axis=1)
    counts = jnp.sum(slot_table, axis=1)
    highest = lax.Precision.HIGHEST
    dot = lambda a, b: jnp.dot(a, b, precision=highest)
    moments = dot(right_side, slot_table.T)
    own_part = dot(right_side * self_diag[None, :], slot_table.T) + dot(self_trans, moments)
    moments = dot(far_trans, moments)
    g = group_count
    filler = jnp.zeros((g, g), jnp.float32)
    payload = jnp.concatenate(
        [
            jnp.concatenate([moments, own_part, jnp.zeros_like(moments)], axis=1),
            select_mat,
            jnp.concatenate([counts[:, None], jnp.zeros((g, 3 * g - 1), jnp.float32)], axis=1),
        ],
        axis=0,
    )
    rows = moments.shape[0]
    payload, moments = lax.optimization_barrier((payload, moments))
    below = shifted(payload, DEVICES, 1)
    above = shifted(payload, DEVICES, -1)
    two_below = shifted(moments, DEVICES, 2)
    two_above = shifted(moments, DEVICES, -2)
    unpack = lambda block: (
        block[:rows, :g],
        block[:rows, g : 2 * g],
        block[rows : rows + g],
        block[rows + g :, 0],
    )
    moments_below, part_below, select_below, counts_below = unpack(below)
    moments_above, part_above, select_above, counts_above = unpack(above)
    wide = jnp.concatenate([two_below, moments_below, moments, moments_above, two_above], axis=1)
    wide_select = jnp.concatenate(
        [
            jnp.concatenate([select_below, filler, filler], axis=1),
            jnp.concatenate([filler, select_mat, filler], axis=1),
            jnp.concatenate([filler, filler, select_above], axis=1),
        ],
        axis=0,
    )
    local_near = dot(wide, wide_select.T)
    near_counts = jnp.concatenate([counts_below, counts, counts_above])
    near_part = jnp.concatenate([part_below, own_part, part_above], axis=1)
    near_moments = near_part + near_counts[None, :] * local_near
    own_local = lax.optimization_barrier(local_part(right_side, self_diag, self_trans))
    first = own_local + dot(local_near[:, g : 2 * g], slot_table)
    local_next = dot(far_trans, dot(near_moments, select_mat.T))
    second = local_part(first, self_diag, self_trans) + dot(local_next, slot_table)
    krylov = (right_side, first, second)
    columns_sums = jnp.stack([jnp.sum(krylov[i] * krylov[j], axis=0) for i, j in GRAM_PAIRS])
    partials = jnp.sum(columns_sums, axis=1)
    totals = all_sum(partials)
    lanes = lax.optimization_barrier(jnp.broadcast_to(totals[:, None], (len(GRAM_PAIRS), 128)))
    g00, g01, g02, g11, g12, g22 = [lanes[k] for k in range(len(GRAM_PAIRS))]
    beta_norm = jnp.sqrt(g00)
    h00 = g01 / g00
    h10 = jnp.sqrt(g11 / g00 - h00 * h00)
    scale = beta_norm * h10
    h01 = (g02 - h00 * g01) / (beta_norm * scale)
    h11 = (g12 - h00 * g11 - h00 * g02 + h00 * h00 * g01) / (scale * scale)
    ww1 = (g22 - 2.0 * h00 * g12 + h00 * h00 * g11) / (scale * scale)
    h21 = jnp.sqrt(ww1 - h01 * h01 - h11 * h11)
    zero = jnp.zeros_like(h00)
    y0, y1 = least_squares(((h00, h01), (h10, h11), (zero, h21)), beta_norm)
    c1 = y1 / scale
    c0 = y0 / beta_norm - c1 * h00
    c0, c1 = lax.optimization_barrier((c0, c1))
    return c0[0] * right_side + c1[0] * first


def solution(mesh):
    placed = (
        P(None, DEVICES),
        P(DEVICES),
        P(DEVICES, None),
        P(DEVICES, None),
        P(DEVICES),
        P(),
        P(),
    )
    return jax.shard_map(
        on_device, mesh=mesh, in_specs=placed, out_specs=P(None, DEVICES), check_vma=False
    )
```
